32 devices in a mesh: groups: 2 (over x), tile: 16 (over z, y, core).
Axes of the slice: x: 2, y: 2, z: 4, core: 2. Of those that a mesh axis runs over, the one named last changes fastest.
Arguments:
- frames: bfloat16 [32, 16, 64, 384], P(('groups', 'tile')), parts along dimension 0, may hold values from -6 to 6
- norm_gain: float32 [384], replicated, may hold values from 0.1 to 1.9
- conv_weight: bfloat16 [3, 3, 3, 384, 384], replicated, may hold values from -0.0625 to 0.0625
- conv_bias: float32 [384], replicated, may hold values from -3 to 3
- up_weight: bfloat16 [384, 4, 4, 192], replicated, may hold values from -0.15625 to 0.15625
- up_bias: float32 [192], replicated, may hold values from -3 to 3
- continues: int32 [8], P('groups'), parts along dimension 0, may hold values from 0 to 1, as said below
- row_extent: int32 [32], P(('groups', 'tile')), parts along dimension 0, may hold values from 1 to 16, as said below
- col_extent: int32 [32], P(('groups', 'tile')), parts along dimension 0, may hold values from 1 to 64, as said below
Outputs:
- upsampled: bfloat16 [32, 32, 128, 192], P(('groups', 'tile')), parts along dimension 0
The draws below stay inside these ranges and needn't reach their ends.
There are 2 independent parts, one for each index of `groups`. The reference program is written for one: setup_inputs(seed, part) draws one part's arguments, and reference() takes and returns one part's arrays. A program takes and returns all parts, laid end to end along the dimension named above; an argument that names none is the same for every part. Nothing has to cross between parts.
Inputs may be any that keep to these rules, and one draw needn't show every extreme that they name: continues[0] and continues[1] are 0; at least one later entry is 1. The valid cells of every latent frame form one rectangle at its first rows and columns, the same for all latent frames; row_extent is 16 except in tile row 1. col_extent is 64 except in tile column 1, in the same rectangle.
All inputs are finite; a program needn't handle non-finite values.
Results may differ from the reference program's by a relative error of at most 0.0048.
Values may be sent and summed in bfloat16 or wider, within the bound.
No kernel may reach another device: no remote copies, remote signals or barrier semaphores. Data moves between devices by JAX's collectives and lax.ppermute only.
A program may use at most 128 MiB of HBM per device.

```python
import jax
import jax.numpy as jnp
from jax import lax

C = 384
CO = 192
HT = 16
WT = 64
TX = 2
LATENTS = 4
TY = 2
TILES = 16


def draw_continues(key, part):
    base = jax.random.fold_in(key, part)
    indices = jnp.arange(LATENTS, dtype=jnp.int32)
    random_bits = jax.random.randint(jax.random.fold_in(base, 11), (LATENTS,), 0, 2)
    forced = jax.random.randint(jax.random.fold_in(base, 13), (), 2, LATENTS)
    flags = jnp.where(indices == forced, 1, random_bits)
    return jnp.where(indices >= 2, flags, 0).astype(jnp.int32)


def tile_extent(key, part, extent_size, tiles_across, stride, salt_value):
    base = jax.random.fold_in(key, part)
    extent = jax.random.randint(jax.random.fold_in(base, salt_value), (), (tiles_across - 1) * extent_size + 1, tiles_across * extent_size + 1)
    indices = jnp.arange(TILES, dtype=jnp.int32)
    tile_pos = indices % (TX * TY) // stride % tiles_across
    return jnp.clip(extent - tile_pos * extent_size, 0, extent_size).astype(jnp.int32)


def draw_row_extent(key, part):
    return tile_extent(key, part, HT, TY, TX, 5)


def draw_col_extent(key, part):
    return tile_extent(key, part, WT, TX, 1, 7)


def levels(key, shape, cuts, smallest, largest):
    gain = 1.0
    for dim, blocks in cuts:
        heights = jax.random.uniform(jax.random.fold_in(jax.random.fold_in(key, 6), dim), (blocks,), jnp.float32, smallest / len(cuts), largest / len(cuts))
        gain = gain * jnp.repeat(jnp.exp(heights), shape[dim] // blocks).reshape((-1,) + (1,) * (len(shape) - 1 - dim))
    return gain


def bell_draw(own_key, dims, width, reach, pieces=(), held_as=jnp.bfloat16):
    level = levels(own_key, dims, pieces, -0.22, 0.18) if pieces else 1.0
    array = jax.random.normal(own_key, dims, jnp.float32) * width * level
    return jnp.minimum(jnp.maximum(array, -reach), reach).astype(held_as)


def setup_inputs(seed: int = 0, part: int = 0) -> dict:
    streams_of = jax.random.split(jax.random.key(seed), 10)
    part_keys = jax.random.split(jax.random.fold_in(streams_of[9], part), 10)
    return {
        "frames": bell_draw(part_keys[0], (TILES, HT, WT, C), 1.0, 6.0, ((0, 16),)),
        "norm_gain": jnp.clip(1.0 + 0.18 * jax.random.normal(streams_of[1], (C,), jnp.float32), 0.1, 1.9),
        "conv_weight": bell_draw(streams_of[2], (3, 3, 3, C, C), (27 * C) ** -0.5, 0.0625),
        "conv_bias": bell_draw(streams_of[3], (C,), 0.5, 3.0, (), jnp.float32),
        "up_weight": bell_draw(streams_of[4], (C, 4, 4, CO), (4 * C) ** -0.5, 0.15625),
        "up_bias": bell_draw(streams_of[5], (CO,), 0.5, 3.0, (), jnp.float32),
        "continues": draw_continues(jax.random.fold_in(jax.random.fold_in(streams_of[9], part), 71), part),
        "row_extent": draw_row_extent(jax.random.fold_in(jax.random.fold_in(streams_of[9], part), 71), part),
        "col_extent": draw_col_extent(jax.random.fold_in(jax.random.fold_in(streams_of[9], part), 71), part),
    }


EPSILON = 1e-06

def to_frames(tiles):
    trailing = tiles.shape[3:]
    height = tiles.shape[1]
    breadth = tiles.shape[2]
    tiled = tiles.reshape((LATENTS, TY, TX, height, breadth) + trailing)
    tiled = jnp.swapaxes(tiled, 2, 3)
    return tiled.reshape((LATENTS, TY * height, TX * breadth) + trailing)

def to_tiles(whole):
    trailing = whole.shape[3:]
    height = whole.shape[1] // TY
    breadth = whole.shape[2] // TX
    tiled = whole.reshape((LATENTS, TY, height, TX, breadth) + trailing)
    tiled = jnp.swapaxes(tiled, 2, 3)
    return tiled.reshape((TILES, height, breadth) + trailing)

def activate(values, norm_gain, valid_cells):
    square = lax.optimization_barrier(jnp.mean(values * values, axis=-1, keepdims=True))
    scaled = values * lax.rsqrt(square + EPSILON) * norm_gain
    return (jax.nn.silu(scaled) * valid_cells[..., None]).astype(jnp.bfloat16)

def parity_planes(products):
    planes = []
    for row_par in range(2):
        plane_row = []
        for col_par in range(2):
            terms = []
            for row_tap in range(2):
                for col_tap in range(2):
                    piece = products[:, :, row_par + 2 * row_tap, col_par + 2 * col_tap]
                    terms.append(jnp.pad(piece, ((row_tap, 1 - row_tap), (col_tap, 1 - col_tap), (0, 0))))
            plane_row.append(terms[0] + terms[1] + terms[2] + terms[3])
        planes.append(jnp.stack(plane_row))
    return jnp.stack(planes)

def alternate(planes, offset, height, breadth):
    row_parts = []
    for row_par in range(2):
        col_parts = []
        for col_par in range(2):
            col_parts.append(planes[1 - row_par, 1 - col_par, offset + row_par:offset + row_par + height, offset + col_par:offset + col_par + breadth])
        row_parts.append(jnp.stack(col_parts, axis=2))
    woven = jnp.stack(row_parts, axis=1)
    return woven.reshape(2 * height, 2 * breadth, woven.shape[-1])

def reference(frames, norm_gain, conv_weight, conv_bias, up_weight, up_bias, continues, row_extent, col_extent):
    row_ids = jnp.arange(HT, dtype=jnp.int32)
    col_ids = jnp.arange(WT, dtype=jnp.int32)
    tile_valid = ((row_ids[None, :, None] < row_extent[:, None, None]) & (col_ids[None, None, :] < col_extent[:, None, None])).astype(jnp.float32)
    valid_cells = to_frames(tile_valid)
    values = to_frames(frames).astype(jnp.float32)
    active = activate(values, norm_gain, valid_cells)
    empty_frame = jnp.zeros_like(active[:1])
    last_frame = jnp.concatenate([empty_frame, active[:-1]], axis=0)
    before = jnp.concatenate([empty_frame, empty_frame, active[:-2]], axis=0)[:LATENTS]
    flag_list = continues.astype(jnp.bfloat16)
    before = before * flag_list[:, None, None, None]
    stacked = jnp.stack([before, last_frame, active], axis=1)
    padded = jnp.pad(stacked, ((0, 0), (0, 0), (1, 1), (1, 1), (0, 0)))
    conv_out = lax.conv_general_dilated(padded, conv_weight, (1, 1, 1), 'VALID', dimension_numbers=('NDHWC', 'DHWIO', 'NDHWC'), preferred_element_type=jnp.float32)[:, 0]
    hidden = ((values + conv_out + conv_bias) * valid_cells[..., None]).astype(jnp.bfloat16)
    weight_flat = up_weight.reshape(C, 16 * CO)
    outputs = []
    for position in range(LATENTS):
        products = jnp.dot(hidden[position].reshape(-1, C), weight_flat, preferred_element_type=jnp.float32)
        products = products.reshape(TY * HT, TX * WT, 4, 4, CO)
        planes = parity_planes(products)
        outputs.append(alternate(planes, 0, TY * HT, TX * WT))
    summed = jnp.stack(outputs)
    wide_valid = jnp.repeat(jnp.repeat(valid_cells, 2, axis=1), 2, axis=2)
    upsampled = ((summed + up_bias) * wide_valid[..., None]).astype(jnp.bfloat16)
    return to_tiles(upsampled)
```

```python
import jax
import jax.numpy as jnp
from jax import lax
from jax.sharding import PartitionSpec as P

TX = 2


EPSILON = 1e-06


def activate(values, norm_gain, valid_cells):
    square = jnp.mean(values * values, axis=-1, keepdims=True)
    scaled = values * lax.rsqrt(square + EPSILON) * norm_gain
    return (jax.nn.silu(scaled) * valid_cells[..., None]).astype(jnp.bfloat16)


def latent_step(block, frame_tiles):
    length = lax.axis_size("tile")
    route = [(i, i + frame_tiles) for i in range(length - frame_tiles)]
    return lax.ppermute(block, "tile", route)


def neighbour_shift(block, frame_tiles, step_rows, step_cols):
    length = lax.axis_size("tile")
    tile_rows = frame_tiles // TX
    route = []
    for i in range(length):
        latent, rest = divmod(i, frame_tiles)
        ty, tx = divmod(rest, TX)
        ty2, tx2 = ty + step_rows, tx + step_cols
        if 0 <= ty2 < tile_rows and 0 <= tx2 < TX:
            route.append((i, latent * frame_tiles + ty2 * TX + tx2))
    return lax.ppermute(block, "tile", route)


def widen(cells, frame_tiles):
    shift = lambda piece, r, c: neighbour_shift(piece, frame_tiles, r, c)
    top = shift(cells[-1:], 1, 0)
    bottom = shift(cells[:1], -1, 0)
    left = shift(cells[:, -1:], 0, 1)
    right = shift(cells[:, :1], 0, -1)
    top_left = shift(cells[-1:, -1:], 1, 1)
    top_right = shift(cells[-1:, :1], 1, -1)
    bottom_left = shift(cells[:1, -1:], -1, 1)
    bottom_right = shift(cells[:1, :1], -1, -1)
    upper = jnp.concatenate([top_left, top, top_right], axis=1)
    middle = jnp.concatenate([left, cells, right], axis=1)
    lower = jnp.concatenate([bottom_left, bottom, bottom_right], axis=1)
    return jnp.concatenate([upper, middle, lower], axis=0)


def conv2d(widened, kernel):
    return lax.conv_general_dilated(
        widened[None],
        kernel,
        (1, 1),
        "VALID",
        dimension_numbers=("NHWC", "HWIO", "NHWC"),
        preferred_element_type=jnp.float32,
    )[0]


def up_kernels(up_weight):
    channels, _, _, out_channels = up_weight.shape
    zero = jnp.zeros((channels, out_channels), up_weight.dtype)
    row_taps = ((3, 1), (2, 0))
    col_taps = ((3, None), (1, 2), (None, 0))
    kernels = []
    for row_par in range(2):
        rows = []
        for ky in row_taps[row_par]:
            cols = []
            for kx_pair in col_taps:
                halves = [zero if kx is None else up_weight[:, ky, kx, :] for kx in kx_pair]
                cols.append(jnp.concatenate(halves, axis=1))
            rows.append(jnp.stack(cols))
        kernels.append(jnp.stack(rows))
    return kernels


def body(
    frames, norm_gain, conv_weight, conv_bias, up_weight, up_bias, continues, row_extent, col_extent
):
    latents = continues.shape[0]
    frame_tiles = lax.axis_size("tile") // latents
    position = lax.axis_index("tile")
    latent_id = position // frame_tiles
    height = frames.shape[1]
    breadth = frames.shape[2]
    out_channels = up_weight.shape[3]
    row_ids = jnp.arange(height, dtype=jnp.int32)
    col_ids = jnp.arange(breadth, dtype=jnp.int32)
    valid_cells = ((row_ids[:, None] < row_extent[0]) & (col_ids[None, :] < col_extent[0])).astype(
        jnp.float32
    )
    raw = frames[0]
    raw_last = latent_step(raw, frame_tiles)
    raw_before = latent_step(raw_last, frame_tiles)

    values = raw.astype(jnp.float32)
    active = activate(values, norm_gain, valid_cells)
    conv_out = conv2d(widen(active, frame_tiles), conv_weight[2])

    last_frame = activate(raw_last.astype(jnp.float32), norm_gain, valid_cells)
    conv_out = conv_out + conv2d(widen(last_frame, frame_tiles), conv_weight[1])

    slots = jnp.arange(latents, dtype=jnp.int32)
    flag_second = jnp.sum(jnp.where(slots == latent_id, continues, 0)).astype(jnp.bfloat16)
    before = activate(raw_before.astype(jnp.float32), norm_gain, valid_cells) * flag_second
    conv_out = conv_out + conv2d(widen(before, frame_tiles), conv_weight[0])

    hidden = ((values + conv_out + conv_bias) * valid_cells[..., None]).astype(jnp.bfloat16)
    hidden_wide = widen(hidden, frame_tiles)
    kernels = up_kernels(up_weight)
    bias_pair = jnp.concatenate([up_bias, up_bias])
    planes = []
    for row_par in range(2):
        summed = conv2d(hidden_wide[row_par : row_par + height + 1], kernels[row_par])
        planes.append(((summed + bias_pair) * valid_cells[..., None]).astype(jnp.bfloat16))
    woven = jnp.stack(planes, axis=1)
    upsampled = woven.reshape(2 * height, 2 * breadth, out_channels)
    return upsampled[None]


def solution(mesh):
    return jax.shard_map(
        body,
        mesh=mesh,
        in_specs=(
            P(("groups", "tile"), None, None, None),
            P(),
            P(),
            P(),
            P(),
            P(),
            P("groups"),
            P(("groups", "tile")),
            P(("groups", "tile")),
        ),
        out_specs=P(("groups", "tile"), None, None, None),
        check_vma=False,
    )
```

```python
import jax
import jax.numpy as jnp
from jax import lax
from jax.sharding import PartitionSpec as P

TX = 2


EPSILON = 1e-06

DIRECTIONS = ((1, 0), (-1, 0), (0, 1), (0, -1), (1, 1), (-1, -1), (1, -1), (-1, 1))


def activate(values, norm_gain, valid_cells):
    square = jnp.mean(values * values, axis=-1, keepdims=True)
    scaled = values * lax.rsqrt(square + EPSILON) * norm_gain
    return (jax.nn.silu(scaled) * valid_cells[..., None]).astype(jnp.bfloat16)


def latent_step(block, frame_tiles):
    length = lax.axis_size("tile")
    route = [(i, i + frame_tiles) for i in range(length - frame_tiles)]
    return lax.ppermute(block, "tile", route)


def direction_pairs(frame_tiles, step):
    length = lax.axis_size("tile")
    tile_rows = frame_tiles // TX
    step_rows, step_cols = step
    pairs = []
    for i in range(length):
        latent, rest = divmod(i, frame_tiles)
        ty, tx = divmod(rest, TX)
        ty2, tx2 = ty + step_rows, tx + step_cols
        if 0 <= ty2 < tile_rows and 0 <= tx2 < TX:
            pairs.append((i, latent * frame_tiles + ty2 * TX + tx2))
    return pairs


def direction_groups(frame_tiles):
    groups = []
    for step in DIRECTIONS:
        pairs = direction_pairs(frame_tiles, step)
        kind = (abs(step[0]), abs(step[1]))
        for group in groups:
            if group["kind"] != kind:
                continue
            sources = {s for s, _ in group["pairs"]}
            targets = {t for _, t in group["pairs"]}
            if sources.isdisjoint(s for s, _ in pairs) and targets.isdisjoint(t for _, t in pairs):
                group["steps"].append(step)
                group["pairs"] = group["pairs"] + pairs
                break
        else:
            groups.append({"kind": kind, "steps": [step], "pairs": pairs})
    return groups


def piece_for(cells, step):
    rows = {1: slice(-1, None), -1: slice(0, 1), 0: slice(None)}[step[0]]
    cols = {1: slice(-1, None), -1: slice(0, 1), 0: slice(None)}[step[1]]
    return cells[rows, cols]


def halo_exchange(cells, frame_tiles):
    length = lax.axis_size("tile")
    position = lax.axis_index("tile")
    received = {}
    for group in direction_groups(frame_tiles):
        steps = group["steps"]
        if len(steps) == 1:
            received[steps[0]] = lax.ppermute(piece_for(cells, steps[0]), "tile", group["pairs"])
            continue
        send_id = [-1] * length
        recv_id = [-1] * length
        for k, step in enumerate(steps):
            for s, t in direction_pairs(frame_tiles, step):
                send_id[s] = k
                recv_id[t] = k
        my_send = jnp.asarray(send_id, jnp.int32)[position]
        my_recv = jnp.asarray(recv_id, jnp.int32)[position]
        piece = piece_for(cells, steps[0])
        for k in range(1, len(steps)):
            piece = jnp.where(my_send == k, piece_for(cells, steps[k]), piece)
        got = lax.ppermute(piece, "tile", group["pairs"])
        for k, step in enumerate(steps):
            received[step] = jnp.where(my_recv == k, got, jnp.zeros_like(got))
    upper = jnp.concatenate([received[(1, 1)], received[(1, 0)], received[(1, -1)]], axis=1)
    middle = jnp.concatenate([received[(0, 1)], cells, received[(0, -1)]], axis=1)
    lower = jnp.concatenate([received[(-1, 1)], received[(-1, 0)], received[(-1, -1)]], axis=1)
    return jnp.concatenate([upper, middle, lower], axis=0)


def conv2d(widened, kernel):
    return lax.conv_general_dilated(
        widened[None],
        kernel,
        (1, 1),
        "VALID",
        dimension_numbers=("NHWC", "HWIO", "NHWC"),
        preferred_element_type=jnp.float32,
    )[0]


def up_kernels(up_weight):
    channels, _, _, out_channels = up_weight.shape
    zero = jnp.zeros((channels, out_channels), up_weight.dtype)
    row_taps = ((3, 1), (2, 0))
    col_taps = ((3, None), (1, 2), (None, 0))
    kernels = []
    for row_par in range(2):
        rows = []
        for ky in row_taps[row_par]:
            cols = []
            for kx_pair in col_taps:
                halves = [zero if kx is None else up_weight[:, ky, kx, :] for kx in kx_pair]
                cols.append(jnp.concatenate(halves, axis=1))
            rows.append(jnp.stack(cols))
        kernels.append(jnp.stack(rows))
    return kernels


def body(
    frames, norm_gain, conv_weight, conv_bias, up_weight, up_bias, continues, row_extent, col_extent
):
    latents = continues.shape[0]
    frame_tiles = lax.axis_size("tile") // latents
    position = lax.axis_index("tile")
    latent_id = position // frame_tiles
    height = frames.shape[1]
    breadth = frames.shape[2]
    out_channels = up_weight.shape[3]
    rows_in = row_extent[0]
    cols_in = col_extent[0]
    row_ids = jnp.arange(height, dtype=jnp.int32)
    col_ids = jnp.arange(breadth, dtype=jnp.int32)
    valid_cells = ((row_ids[:, None] < rows_in) & (col_ids[None, :] < cols_in)).astype(jnp.float32)
    wide_rows = jnp.arange(-1, height + 1, dtype=jnp.int32)
    wide_cols = jnp.arange(-1, breadth + 1, dtype=jnp.int32)
    row_ok = (wide_rows < rows_in) | ((wide_rows == height) & (rows_in == height))
    col_ok = (wide_cols < cols_in) | ((wide_cols == breadth) & (cols_in == breadth))
    wide_valid = (row_ok[:, None] & col_ok[None, :]).astype(jnp.float32)

    raw = frames[0]
    raw_wide = halo_exchange(raw, frame_tiles)
    raw_last = latent_step(raw_wide, frame_tiles)
    raw_before = latent_step(raw_last, frame_tiles)

    active = activate(raw_wide.astype(jnp.float32), norm_gain, wide_valid)
    conv_out = conv2d(active, conv_weight[2])

    last_frame = activate(raw_last.astype(jnp.float32), norm_gain, wide_valid)
    conv_out = conv_out + conv2d(last_frame, conv_weight[1])

    slots = jnp.arange(latents, dtype=jnp.int32)
    flag_second = jnp.sum(jnp.where(slots == latent_id, continues, 0)).astype(jnp.bfloat16)
    before = activate(raw_before.astype(jnp.float32), norm_gain, wide_valid) * flag_second
    conv_out = conv_out + conv2d(before, conv_weight[0])

    values = raw.astype(jnp.float32)
    hidden = ((values + conv_out + conv_bias) * valid_cells[..., None]).astype(jnp.bfloat16)
    hidden_wide = halo_exchange(hidden, frame_tiles)
    kernels = up_kernels(up_weight)
    bias_pair = jnp.concatenate([up_bias, up_bias])
    planes = []
    for row_par in range(2):
        summed = conv2d(hidden_wide[row_par : row_par + height + 1], kernels[row_par])
        planes.append(((summed + bias_pair) * valid_cells[..., None]).astype(jnp.bfloat16))
    woven = jnp.stack(planes, axis=1)
    upsampled = woven.reshape(2 * height, 2 * breadth, out_channels)
    return upsampled[None]


def solution(mesh):
    return jax.shard_map(
        body,
        mesh=mesh,
        in_specs=(
            P(("groups", "tile"), None, None, None),
            P(),
            P(),
            P(),
            P(),
            P(),
            P("groups"),
            P(("groups", "tile")),
            P(("groups", "tile")),
        ),
        out_specs=P(("groups", "tile"), None, None, None),
        check_vma=False,
    )
```

```python
import jax
import jax.numpy as jnp
from jax import lax
from jax.sharding import PartitionSpec as P


TX = 2


EPSILON = 1e-06

DIRECTIONS = ((1, 0), (-1, 0), (0, 1), (0, -1), (1, 1), (-1, -1), (1, -1), (-1, 1))


def activate(values, norm_gain, valid_cells):
    square = jnp.mean(values * values, axis=-1, keepdims=True)
    scaled = values * lax.rsqrt(square + EPSILON) * norm_gain
    return (jax.nn.silu(scaled) * valid_cells[..., None]).astype(jnp.bfloat16)


def latent_step(block, frame_tiles):
    length = lax.axis_size("tile")
    route = [(i, i + frame_tiles) for i in range(length - frame_tiles)]
    return lax.ppermute(block, "tile", route)


def direction_pairs(frame_tiles, step):
    length = lax.axis_size("tile")
    tile_rows = frame_tiles // TX
    step_rows, step_cols = step
    pairs = []
    for i in range(length):
        latent, rest = divmod(i, frame_tiles)
        ty, tx = divmod(rest, TX)
        ty2, tx2 = ty + step_rows, tx + step_cols
        if 0 <= ty2 < tile_rows and 0 <= tx2 < TX:
            pairs.append((i, latent * frame_tiles + ty2 * TX + tx2))
    return pairs


def direction_groups(frame_tiles):
    groups = []
    for step in DIRECTIONS:
        pairs = direction_pairs(frame_tiles, step)
        kind = (abs(step[0]), abs(step[1]))
        for group in groups:
            if group["kind"] != kind:
                continue
            sources = {s for s, _ in group["pairs"]}
            targets = {t for _, t in group["pairs"]}
            if sources.isdisjoint(s for s, _ in pairs) and targets.isdisjoint(t for _, t in pairs):
                group["steps"].append(step)
                group["pairs"] = group["pairs"] + pairs
                break
        else:
            groups.append({"kind": kind, "steps": [step], "pairs": pairs})
    return groups


def in_frame(ty, tx, tile_rows):
    return (ty >= 0) & (ty < tile_rows) & (tx >= 0) & (tx < TX)


def halo_exchange(cells, frame_tiles):
    tile_rows = frame_tiles // TX
    position = lax.axis_index("tile")
    ty = position % frame_tiles // TX
    tx = position % TX
    height, breadth, channels = cells.shape
    received = {}
    for group in direction_groups(frame_tiles):
        steps = group["steps"]
        row_at = jnp.int32(0)
        col_at = jnp.int32(0)
        for step in steps:
            sends = in_frame(ty + step[0], tx + step[1], tile_rows)
            row_at = jnp.where(sends, height - 1 if step[0] == 1 else 0, row_at)
            col_at = jnp.where(sends, breadth - 1 if step[1] == 1 else 0, col_at)
        sizes = (1 if steps[0][0] else height, 1 if steps[0][1] else breadth, channels)
        piece = lax.dynamic_slice(cells, (row_at, col_at, jnp.int32(0)), sizes)
        got = lax.ppermute(piece, "tile", group["pairs"])
        for step in steps:
            if len(steps) == 1:
                received[step] = got
            else:
                gets = in_frame(ty - step[0], tx - step[1], tile_rows)
                received[step] = jnp.where(gets, got, jnp.zeros_like(got))
    upper = jnp.concatenate([received[(1, 1)], received[(1, 0)], received[(1, -1)]], axis=1)
    middle = jnp.concatenate([received[(0, 1)], cells, received[(0, -1)]], axis=1)
    lower = jnp.concatenate([received[(-1, 1)], received[(-1, 0)], received[(-1, -1)]], axis=1)
    return jnp.concatenate([upper, middle, lower], axis=0)


def conv2d(widened, kernel):
    return lax.conv_general_dilated(
        widened[None],
        kernel,
        (1, 1),
        "VALID",
        dimension_numbers=("NHWC", "HWIO", "NHWC"),
        preferred_element_type=jnp.float32,
    )[0]


def up_kernels(up_weight):
    channels, _, _, out_channels = up_weight.shape
    zero = jnp.zeros((channels, out_channels), up_weight.dtype)
    row_taps = ((3, 1), (2, 0))
    col_taps = ((3, None), (1, 2), (None, 0))
    kernels = []
    for row_par in range(2):
        rows = []
        for ky in row_taps[row_par]:
            cols = []
            for kx_pair in col_taps:
                halves = [zero if kx is None else up_weight[:, ky, kx, :] for kx in kx_pair]
                cols.append(jnp.concatenate(halves, axis=1))
            rows.append(jnp.stack(cols))
        kernels.append(jnp.stack(rows))
    return kernels


def body(
    frames, norm_gain, conv_weight, conv_bias, up_weight, up_bias, continues, row_extent, col_extent
):
    latents = continues.shape[0]
    frame_tiles = lax.axis_size("tile") // latents
    position = lax.axis_index("tile")
    latent_id = position // frame_tiles
    height = frames.shape[1]
    breadth = frames.shape[2]
    out_channels = up_weight.shape[3]
    rows_in = row_extent[0]
    cols_in = col_extent[0]
    row_ids = jnp.arange(height, dtype=jnp.int32)
    col_ids = jnp.arange(breadth, dtype=jnp.int32)
    valid_cells = ((row_ids[:, None] < rows_in) & (col_ids[None, :] < cols_in)).astype(jnp.float32)
    wide_rows = jnp.arange(-1, height + 1, dtype=jnp.int32)
    wide_cols = jnp.arange(-1, breadth + 1, dtype=jnp.int32)
    row_ok = (wide_rows < rows_in) | ((wide_rows == height) & (rows_in == height))
    col_ok = (wide_cols < cols_in) | ((wide_cols == breadth) & (cols_in == breadth))
    wide_valid = (row_ok[:, None] & col_ok[None, :]).astype(jnp.float32)

    raw = frames[0]
    raw_wide = halo_exchange(raw, frame_tiles)
    raw_last = latent_step(raw_wide, frame_tiles)
    kernels = up_kernels(up_weight)
    active = activate(raw_wide.astype(jnp.float32), norm_gain, wide_valid)
    conv_own = lax.optimization_barrier(conv2d(active, conv_weight[2]))
    raw_before = latent_step(raw_last, frame_tiles)
    last_frame = activate(raw_last.astype(jnp.float32), norm_gain, wide_valid)
    conv_last = conv2d(last_frame, conv_weight[1]) + conv_own

    slots = jnp.arange(latents, dtype=jnp.int32)
    flag_second = jnp.sum(jnp.where(slots == latent_id, continues, 0)).astype(jnp.bfloat16)
    before = activate(raw_before.astype(jnp.float32), norm_gain, wide_valid) * flag_second
    conv_out = conv2d(before, conv_weight[0]) + conv_last

    values = raw.astype(jnp.float32)
    hidden = ((values + conv_out + conv_bias) * valid_cells[..., None]).astype(jnp.bfloat16)
    hidden_wide = halo_exchange(hidden, frame_tiles)
    bias_pair = jnp.concatenate([up_bias, up_bias])
    planes = []
    for row_par in range(2):
        summed = conv2d(hidden_wide[row_par : row_par + height + 1], kernels[row_par])
        planes.append(((summed + bias_pair) * valid_cells[..., None]).astype(jnp.bfloat16))
    woven = jnp.stack(planes, axis=1)
    upsampled = woven.reshape(2 * height, 2 * breadth, out_channels)
    return upsampled[None]


def solution(mesh):
    return jax.shard_map(
        body,
        mesh=mesh,
        in_specs=(
            P(("groups", "tile"), None, None, None),
            P(),
            P(),
            P(),
            P(),
            P(),
            P("groups"),
            P(("groups", "tile")),
            P(("groups", "tile")),
        ),
        out_specs=P(("groups", "tile"), None, None, None),
        check_vma=False,
    )
```

```python
import jax
import numpy as np
import jax.numpy as jnp
from jax import lax
from jax.sharding import PartitionSpec as P


TX = 2


EPSILON = 1e-06

DIRECTIONS = ((1, 0), (-1, 0), (0, 1), (0, -1), (1, 1), (-1, -1), (1, -1), (-1, 1))


def activate(values, norm_gain, valid_cells):
    square = jnp.mean(values * values, axis=-1, keepdims=True)
    scaled = values * lax.rsqrt(square + EPSILON) * norm_gain
    return (jax.nn.silu(scaled) * valid_cells[..., None]).astype(jnp.bfloat16)


def latent_step(block, frame_tiles):
    length = lax.axis_size("tile")
    route = [(i, i + frame_tiles) for i in range(length - frame_tiles)]
    return lax.ppermute(block, "tile", route)


def direction_pairs(frame_tiles, step):
    length = lax.axis_size("tile")
    tile_rows = frame_tiles // TX
    step_rows, step_cols = step
    pairs = []
    for i in range(length):
        latent, rest = divmod(i, frame_tiles)
        ty, tx = divmod(rest, TX)
        ty2, tx2 = ty + step_rows, tx + step_cols
        if 0 <= ty2 < tile_rows and 0 <= tx2 < TX:
            pairs.append((i, latent * frame_tiles + ty2 * TX + tx2))
    return pairs


def direction_groups(frame_tiles):
    groups = []
    for step in DIRECTIONS:
        pairs = direction_pairs(frame_tiles, step)
        kind = (abs(step[0]), abs(step[1]))
        for group in groups:
            if group["kind"] != kind:
                continue
            sources = {s for s, _ in group["pairs"]}
            targets = {t for _, t in group["pairs"]}
            if sources.isdisjoint(s for s, _ in pairs) and targets.isdisjoint(t for _, t in pairs):
                group["steps"].append(step)
                group["pairs"] = group["pairs"] + pairs
                break
        else:
            groups.append({"kind": kind, "steps": [step], "pairs": pairs})
    return groups


def in_frame(ty, tx, tile_rows):
    return (ty >= 0) & (ty < tile_rows) & (tx >= 0) & (tx < TX)


def halo_exchange(cells, frame_tiles):
    tile_rows = frame_tiles // TX
    position = lax.axis_index("tile")
    ty = position % frame_tiles // TX
    tx = position % TX
    height, breadth, channels = cells.shape
    received = {}
    for group in direction_groups(frame_tiles):
        steps = group["steps"]
        row_at = jnp.int32(0)
        col_at = jnp.int32(0)
        for step in steps:
            sends = in_frame(ty + step[0], tx + step[1], tile_rows)
            row_at = jnp.where(sends, height - 1 if step[0] == 1 else 0, row_at)
            col_at = jnp.where(sends, breadth - 1 if step[1] == 1 else 0, col_at)
        sizes = (1 if steps[0][0] else height, 1 if steps[0][1] else breadth, channels)
        piece = lax.dynamic_slice(cells, (row_at, col_at, jnp.int32(0)), sizes)
        got = lax.ppermute(piece, "tile", group["pairs"])
        for step in steps:
            if len(steps) == 1:
                received[step] = got
            else:
                gets = in_frame(ty - step[0], tx - step[1], tile_rows)
                received[step] = jnp.where(gets, got, jnp.zeros_like(got))
    upper = jnp.concatenate([received[(1, 1)], received[(1, 0)], received[(1, -1)]], axis=1)
    middle = jnp.concatenate([received[(0, 1)], cells, received[(0, -1)]], axis=1)
    lower = jnp.concatenate([received[(-1, 1)], received[(-1, 0)], received[(-1, -1)]], axis=1)
    return jnp.concatenate([upper, middle, lower], axis=0)


def conv2d(widened, kernel):
    return lax.conv_general_dilated(
        widened[None],
        kernel,
        (1, 1),
        "VALID",
        dimension_numbers=("NHWC", "HWIO", "NHWC"),
        preferred_element_type=jnp.float32,
    )[0]


def up_kernels(up_weight):
    channels, taps_y, taps_x, out_channels = up_weight.shape
    row_taps = ((3, 1), (2, 0))
    col_taps = ((3, None), (1, 2), (None, 0))
    select = np.zeros((2, 2, 3, taps_y * taps_x, 2), np.float32)
    for row_par in range(2):
        for a, ky in enumerate(row_taps[row_par]):
            for b, kx_pair in enumerate(col_taps):
                for col_par, kx in enumerate(kx_pair):
                    if kx is not None:
                        select[row_par, a, b, ky * taps_x + kx, col_par] = 1.0
    select = jnp.asarray(select.reshape(12, taps_y * taps_x, 2), up_weight.dtype)
    flat = up_weight.reshape(channels, taps_y * taps_x, out_channels)
    picked = jnp.einsum("qkr,ckd->qcrd", select, flat, preferred_element_type=jnp.float32)
    picked = picked.astype(up_weight.dtype).reshape(2, 2, 3, channels, 2 * out_channels)
    return [picked[0], picked[1]]


def body(
    frames, norm_gain, conv_weight, conv_bias, up_weight, up_bias, continues, row_extent, col_extent
):
    latents = continues.shape[0]
    frame_tiles = lax.axis_size("tile") // latents
    position = lax.axis_index("tile")
    latent_id = position // frame_tiles
    height = frames.shape[1]
    breadth = frames.shape[2]
    out_channels = up_weight.shape[3]
    rows_in = row_extent[0]
    cols_in = col_extent[0]
    row_ids = jnp.arange(height, dtype=jnp.int32)
    col_ids = jnp.arange(breadth, dtype=jnp.int32)
    valid_cells = ((row_ids[:, None] < rows_in) & (col_ids[None, :] < cols_in)).astype(jnp.float32)
    wide_rows = jnp.arange(-1, height + 1, dtype=jnp.int32)
    wide_cols = jnp.arange(-1, breadth + 1, dtype=jnp.int32)
    row_ok = (wide_rows < rows_in) | ((wide_rows == height) & (rows_in == height))
    col_ok = (wide_cols < cols_in) | ((wide_cols == breadth) & (cols_in == breadth))
    wide_valid = (row_ok[:, None] & col_ok[None, :]).astype(jnp.float32)

    raw = frames[0]
    raw_wide = halo_exchange(raw, frame_tiles)
    raw_last = latent_step(raw_wide, frame_tiles)
    kernels = up_kernels(up_weight)
    active = activate(raw_wide.astype(jnp.float32), norm_gain, wide_valid)
    conv_own = lax.optimization_barrier(conv2d(active, conv_weight[2]))
    raw_before = latent_step(raw_last, frame_tiles)
    last_frame = activate(raw_last.astype(jnp.float32), norm_gain, wide_valid)
    conv_last = conv2d(last_frame, conv_weight[1]) + conv_own

    slots = jnp.arange(latents, dtype=jnp.int32)
    flag_second = jnp.sum(jnp.where(slots == latent_id, continues, 0)).astype(jnp.bfloat16)
    before = activate(raw_before.astype(jnp.float32), norm_gain, wide_valid) * flag_second
    conv_out = conv2d(before, conv_weight[0]) + conv_last

    values = raw.astype(jnp.float32)
    hidden = ((values + conv_out + conv_bias) * valid_cells[..., None]).astype(jnp.bfloat16)
    hidden_wide = halo_exchange(hidden, frame_tiles)
    bias_pair = jnp.concatenate([up_bias, up_bias])
    planes = []
    for row_par in range(2):
        summed = conv2d(hidden_wide[row_par : row_par + height + 1], kernels[row_par])
        planes.append(((summed + bias_pair) * valid_cells[..., None]).astype(jnp.bfloat16))
    woven = jnp.stack(planes, axis=1)
    upsampled = woven.reshape(2 * height, 2 * breadth, out_channels)
    return upsampled[None]


def solution(mesh):
    return jax.shard_map(
        body,
        mesh=mesh,
        in_specs=(
            P(("groups", "tile"), None, None, None),
            P(),
            P(),
            P(),
            P(),
            P(),
            P("groups"),
            P(("groups", "tile")),
            P(("groups", "tile")),
        ),
        out_specs=P(("groups", "tile"), None, None, None),
        check_vma=False,
    )
```

```python
import jax
import numpy as np
import jax.numpy as jnp
from jax import lax
from jax.sharding import PartitionSpec as P


TX = 2


EPSILON = 1e-06

DIRECTIONS = ((1, 0), (-1, 0), (0, 1), (0, -1), (1, 1), (-1, -1), (1, -1), (-1, 1))


def activate(values, norm_gain, valid_cells):
    square = jnp.mean(values * values, axis=-1, keepdims=True)
    scaled = values * lax.rsqrt(square + EPSILON) * norm_gain
    return (jax.nn.silu(scaled) * valid_cells[..., None]).astype(jnp.bfloat16)


def latent_step(block, frame_tiles):
    length = lax.axis_size("tile")
    route = [(i, i + frame_tiles) for i in range(length - frame_tiles)]
    return lax.ppermute(block, "tile", route)


def direction_pairs(frame_tiles, step):
    length = lax.axis_size("tile")
    tile_rows = frame_tiles // TX
    step_rows, step_cols = step
    pairs = []
    for i in range(length):
        latent, rest = divmod(i, frame_tiles)
        ty, tx = divmod(rest, TX)
        ty2, tx2 = ty + step_rows, tx + step_cols
        if 0 <= ty2 < tile_rows and 0 <= tx2 < TX:
            pairs.append((i, latent * frame_tiles + ty2 * TX + tx2))
    return pairs


def direction_groups(frame_tiles):
    groups = []
    for step in DIRECTIONS:
        pairs = direction_pairs(frame_tiles, step)
        kind = (abs(step[0]), abs(step[1]))
        for group in groups:
            if group["kind"] != kind:
                continue
            sources = {s for s, _ in group["pairs"]}
            targets = {t for _, t in group["pairs"]}
            if sources.isdisjoint(s for s, _ in pairs) and targets.isdisjoint(t for _, t in pairs):
                group["steps"].append(step)
                group["pairs"] = group["pairs"] + pairs
                break
        else:
            groups.append({"kind": kind, "steps": [step], "pairs": pairs})
    return groups


def in_frame(ty, tx, tile_rows):
    return (ty >= 0) & (ty < tile_rows) & (tx >= 0) & (tx < TX)


def halo_pieces(cells, frame_tiles, latents_ahead):
    length = lax.axis_size("tile")
    tile_rows = frame_tiles // TX
    position = lax.axis_index("tile")
    ty = position % frame_tiles // TX
    tx = position % TX
    height, breadth, channels = cells.shape
    ahead = latents_ahead * frame_tiles
    received = {}
    for group in direction_groups(frame_tiles):
        steps = group["steps"]
        row_at = jnp.int32(0)
        col_at = jnp.int32(0)
        for step in steps:
            sends = in_frame(ty + step[0], tx + step[1], tile_rows)
            row_at = jnp.where(sends, height - 1 if step[0] == 1 else 0, row_at)
            col_at = jnp.where(sends, breadth - 1 if step[1] == 1 else 0, col_at)
        sizes = (1 if steps[0][0] else height, 1 if steps[0][1] else breadth, channels)
        piece = lax.dynamic_slice(cells, (row_at, col_at, jnp.int32(0)), sizes)
        pairs = [(s, t + ahead) for s, t in group["pairs"] if t + ahead < length]
        got = lax.ppermute(piece, "tile", pairs)
        for step in steps:
            if len(steps) == 1:
                received[step] = got
            else:
                gets = in_frame(ty - step[0], tx - step[1], tile_rows)
                received[step] = jnp.where(gets, got, jnp.zeros_like(got))
    return received


def with_halo(cells, received):
    upper = jnp.concatenate([received[(1, 1)], received[(1, 0)], received[(1, -1)]], axis=1)
    middle = jnp.concatenate([received[(0, 1)], cells, received[(0, -1)]], axis=1)
    lower = jnp.concatenate([received[(-1, 1)], received[(-1, 0)], received[(-1, -1)]], axis=1)
    return jnp.concatenate([upper, middle, lower], axis=0)


def halo_exchange(cells, frame_tiles):
    return with_halo(cells, halo_pieces(cells, frame_tiles, 0))


def conv2d(widened, kernel):
    return lax.conv_general_dilated(
        widened[None],
        kernel,
        (1, 1),
        "VALID",
        dimension_numbers=("NHWC", "HWIO", "NHWC"),
        preferred_element_type=jnp.float32,
    )[0]


def up_kernels(up_weight):
    channels, taps_y, taps_x, out_channels = up_weight.shape
    row_taps = ((3, 1), (2, 0))
    col_taps = ((3, None), (1, 2), (None, 0))
    select = np.zeros((2, 2, 3, taps_y * taps_x, 2), np.float32)
    for row_par in range(2):
        for a, ky in enumerate(row_taps[row_par]):
            for b, kx_pair in enumerate(col_taps):
                for col_par, kx in enumerate(kx_pair):
                    if kx is not None:
                        select[row_par, a, b, ky * taps_x + kx, col_par] = 1.0
    select = jnp.asarray(select.reshape(12, taps_y * taps_x, 2), up_weight.dtype)
    flat = up_weight.reshape(channels, taps_y * taps_x, out_channels)
    picked = jnp.einsum("qkr,ckd->qcrd", select, flat, preferred_element_type=jnp.float32)
    picked = picked.astype(up_weight.dtype).reshape(2, 2, 3, channels, 2 * out_channels)
    return [picked[0], picked[1]]


def body(
    frames, norm_gain, conv_weight, conv_bias, up_weight, up_bias, continues, row_extent, col_extent
):
    latents = continues.shape[0]
    frame_tiles = lax.axis_size("tile") // latents
    position = lax.axis_index("tile")
    latent_id = position // frame_tiles
    height = frames.shape[1]
    breadth = frames.shape[2]
    out_channels = up_weight.shape[3]
    rows_in = row_extent[0]
    cols_in = col_extent[0]
    row_ids = jnp.arange(height, dtype=jnp.int32)
    col_ids = jnp.arange(breadth, dtype=jnp.int32)
    valid_cells = ((row_ids[:, None] < rows_in) & (col_ids[None, :] < cols_in)).astype(jnp.float32)
    wide_rows = jnp.arange(-1, height + 1, dtype=jnp.int32)
    wide_cols = jnp.arange(-1, breadth + 1, dtype=jnp.int32)
    row_ok = (wide_rows < rows_in) | ((wide_rows == height) & (rows_in == height))
    col_ok = (wide_cols < cols_in) | ((wide_cols == breadth) & (cols_in == breadth))
    wide_valid = (row_ok[:, None] & col_ok[None, :]).astype(jnp.float32)

    raw = frames[0]
    raw_last = latent_step(raw, frame_tiles)
    halo_own = halo_pieces(raw, frame_tiles, 0)
    halo_last = halo_pieces(raw, frame_tiles, 1)
    halo_before = halo_pieces(raw, frame_tiles, 2)
    kernels = up_kernels(up_weight)
    raw_wide = with_halo(raw, halo_own)
    active = activate(raw_wide.astype(jnp.float32), norm_gain, wide_valid)
    conv_own = lax.optimization_barrier(conv2d(active, conv_weight[2]))
    raw_before = latent_step(raw_last, frame_tiles)
    last_wide = with_halo(raw_last, halo_last)
    last_frame = activate(last_wide.astype(jnp.float32), norm_gain, wide_valid)
    conv_last = conv2d(last_frame, conv_weight[1]) + conv_own

    slots = jnp.arange(latents, dtype=jnp.int32)
    flag_second = jnp.sum(jnp.where(slots == latent_id, continues, 0)).astype(jnp.bfloat16)
    before_wide = with_halo(raw_before, halo_before)
    before = activate(before_wide.astype(jnp.float32), norm_gain, wide_valid) * flag_second
    conv_out = conv2d(before, conv_weight[0]) + conv_last

    values = raw.astype(jnp.float32)
    hidden = ((values + conv_out + conv_bias) * valid_cells[..., None]).astype(jnp.bfloat16)
    hidden_wide = halo_exchange(hidden, frame_tiles)
    bias_pair = jnp.concatenate([up_bias, up_bias])
    planes = []
    for row_par in range(2):
        summed = conv2d(hidden_wide[row_par : row_par + height + 1], kernels[row_par])
        planes.append(((summed + bias_pair) * valid_cells[..., None]).astype(jnp.bfloat16))
    woven = jnp.stack(planes, axis=1)
    upsampled = woven.reshape(2 * height, 2 * breadth, out_channels)
    return upsampled[None]


def solution(mesh):
    return jax.shard_map(
        body,
        mesh=mesh,
        in_specs=(
            P(("groups", "tile"), None, None, None),
            P(),
            P(),
            P(),
            P(),
            P(),
            P("groups"),
            P(("groups", "tile")),
            P(("groups", "tile")),
        ),
        out_specs=P(("groups", "tile"), None, None, None),
        check_vma=False,
    )
```

```python
import jax
import numpy as np
import jax.numpy as jnp
from jax import lax
from jax.sharding import PartitionSpec as P


TX = 2


EPSILON = 1e-06

DIRECTIONS = ((1, 0), (-1, 0), (0, 1), (0, -1), (1, 1), (-1, -1), (1, -1), (-1, 1))


def activate(values, norm_gain, valid_cells):
    square = jnp.mean(values * values, axis=-1, keepdims=True)
    scaled = values * lax.rsqrt(square + EPSILON) * norm_gain
    return (jax.nn.silu(scaled) * valid_cells[..., None]).astype(jnp.bfloat16)


def latent_step(block, frame_tiles):
    length = lax.axis_size("tile")
    route = [(i, i + frame_tiles) for i in range(length - frame_tiles)]
    return lax.ppermute(block, "tile", route)


def direction_pairs(frame_tiles, step):
    length = lax.axis_size("tile")
    tile_rows = frame_tiles // TX
    step_rows, step_cols = step
    pairs = []
    for i in range(length):
        latent, rest = divmod(i, frame_tiles)
        ty, tx = divmod(rest, TX)
        ty2, tx2 = ty + step_rows, tx + step_cols
        if 0 <= ty2 < tile_rows and 0 <= tx2 < TX:
            pairs.append((i, latent * frame_tiles + ty2 * TX + tx2))
    return pairs


def direction_groups(frame_tiles):
    groups = []
    for step in DIRECTIONS:
        pairs = direction_pairs(frame_tiles, step)
        kind = (abs(step[0]), abs(step[1]))
        for group in groups:
            if group["kind"] != kind:
                continue
            sources = {s for s, _ in group["pairs"]}
            targets = {t for _, t in group["pairs"]}
            if sources.isdisjoint(s for s, _ in pairs) and targets.isdisjoint(t for _, t in pairs):
                group["steps"].append(step)
                group["pairs"] = group["pairs"] + pairs
                break
        else:
            groups.append({"kind": kind, "steps": [step], "pairs": pairs})
    return groups


def in_frame(ty, tx, tile_rows):
    return (ty >= 0) & (ty < tile_rows) & (tx >= 0) & (tx < TX)


def halo_pieces(cells, frame_tiles, latents_ahead):
    length = lax.axis_size("tile")
    tile_rows = frame_tiles // TX
    position = lax.axis_index("tile")
    ty = position % frame_tiles // TX
    tx = position % TX
    height, breadth, channels = cells.shape
    ahead = latents_ahead * frame_tiles
    received = {}
    for group in direction_groups(frame_tiles):
        steps = group["steps"]
        row_at = jnp.int32(0)
        col_at = jnp.int32(0)
        for step in steps:
            sends = in_frame(ty + step[0], tx + step[1], tile_rows)
            row_at = jnp.where(sends, height - 1 if step[0] == 1 else 0, row_at)
            col_at = jnp.where(sends, breadth - 1 if step[1] == 1 else 0, col_at)
        sizes = (1 if steps[0][0] else height, 1 if steps[0][1] else breadth, channels)
        piece = lax.dynamic_slice(cells, (row_at, col_at, jnp.int32(0)), sizes)
        pairs = [(s, t + ahead) for s, t in group["pairs"] if t + ahead < length]
        got = lax.ppermute(piece, "tile", pairs)
        for step in steps:
            if len(steps) == 1:
                received[step] = got
            else:
                gets = in_frame(ty - step[0], tx - step[1], tile_rows)
                received[step] = jnp.where(gets, got, jnp.zeros_like(got))
    return received


def with_halo(cells, received):
    upper = jnp.concatenate([received[(1, 1)], received[(1, 0)], received[(1, -1)]], axis=1)
    middle = jnp.concatenate([received[(0, 1)], cells, received[(0, -1)]], axis=1)
    lower = jnp.concatenate([received[(-1, 1)], received[(-1, 0)], received[(-1, -1)]], axis=1)
    return jnp.concatenate([upper, middle, lower], axis=0)


def halo_exchange(cells, frame_tiles):
    return with_halo(cells, halo_pieces(cells, frame_tiles, 0))


def conv2d(widened, kernel):
    return lax.conv_general_dilated(
        widened[None],
        kernel,
        (1, 1),
        "VALID",
        dimension_numbers=("NHWC", "HWIO", "NHWC"),
        preferred_element_type=jnp.float32,
    )[0]


def up_kernels(up_weight):
    channels, taps_y, taps_x, out_channels = up_weight.shape
    row_taps = ((3, 1), (2, 0))
    col_taps = ((3, None), (1, 2), (None, 0))
    select = np.zeros((2, 2, 3, taps_y * taps_x, 2), np.float32)
    for row_par in range(2):
        for a, ky in enumerate(row_taps[row_par]):
            for b, kx_pair in enumerate(col_taps):
                for col_par, kx in enumerate(kx_pair):
                    if kx is not None:
                        select[row_par, a, b, ky * taps_x + kx, col_par] = 1.0
    select = jnp.asarray(select.reshape(12, taps_y * taps_x, 2), up_weight.dtype)
    flat = up_weight.reshape(channels, taps_y * taps_x, out_channels)
    picked = jnp.einsum("qkr,ckd->qcrd", select, flat, preferred_element_type=jnp.float32)
    picked = picked.astype(up_weight.dtype).reshape(2, 2, 3, channels, 2 * out_channels)
    return [picked[0], picked[1]]


def body(
    frames, norm_gain, conv_weight, conv_bias, up_weight, up_bias, continues, row_extent, col_extent
):
    latents = continues.shape[0]
    frame_tiles = lax.axis_size("tile") // latents
    position = lax.axis_index("tile")
    latent_id = position // frame_tiles
    height = frames.shape[1]
    breadth = frames.shape[2]
    out_channels = up_weight.shape[3]
    rows_in = row_extent[0]
    cols_in = col_extent[0]
    row_ids = jnp.arange(height, dtype=jnp.int32)
    col_ids = jnp.arange(breadth, dtype=jnp.int32)
    valid_cells = ((row_ids[:, None] < rows_in) & (col_ids[None, :] < cols_in)).astype(jnp.float32)
    wide_rows = jnp.arange(-1, height + 1, dtype=jnp.int32)
    wide_cols = jnp.arange(-1, breadth + 1, dtype=jnp.int32)
    row_ok = (wide_rows < rows_in) | ((wide_rows == height) & (rows_in == height))
    col_ok = (wide_cols < cols_in) | ((wide_cols == breadth) & (cols_in == breadth))
    wide_valid = (row_ok[:, None] & col_ok[None, :]).astype(jnp.float32)

    raw = frames[0]
    halo_last = halo_pieces(raw, frame_tiles, 1)
    raw_last = latent_step(raw, frame_tiles)
    halo_own = halo_pieces(raw, frame_tiles, 0)
    kernels = up_kernels(up_weight)
    raw_wide = with_halo(raw, halo_own)
    raw_wide, own_gain, own_valid = lax.optimization_barrier((raw_wide, norm_gain, wide_valid))
    active = activate(raw_wide.astype(jnp.float32), own_gain, own_valid)
    conv_own = lax.optimization_barrier(conv2d(active, conv_weight[2]))
    last_wide = with_halo(raw_last, halo_last)
    before_wide = latent_step(last_wide, frame_tiles)
    last_frame = activate(last_wide.astype(jnp.float32), norm_gain, wide_valid)
    conv_last = conv2d(last_frame, conv_weight[1]) + conv_own

    slots = jnp.arange(latents, dtype=jnp.int32)
    flag_second = jnp.sum(jnp.where(slots == latent_id, continues, 0)).astype(jnp.bfloat16)
    before = activate(before_wide.astype(jnp.float32), norm_gain, wide_valid) * flag_second
    conv_out = conv2d(before, conv_weight[0]) + conv_last

    values = raw.astype(jnp.float32)
    hidden = ((values + conv_out + conv_bias) * valid_cells[..., None]).astype(jnp.bfloat16)
    hidden_wide = halo_exchange(hidden, frame_tiles)
    bias_pair = jnp.concatenate([up_bias, up_bias])
    planes = []
    for row_par in range(2):
        summed = conv2d(hidden_wide[row_par : row_par + height + 1], kernels[row_par])
        planes.append(((summed + bias_pair) * valid_cells[..., None]).astype(jnp.bfloat16))
    woven = jnp.stack(planes, axis=1)
    upsampled = woven.reshape(2 * height, 2 * breadth, out_channels)
    return upsampled[None]


def solution(mesh):
    return jax.shard_map(
        body,
        mesh=mesh,
        in_specs=(
            P(("groups", "tile"), None, None, None),
            P(),
            P(),
            P(),
            P(),
            P(),
            P("groups"),
            P(("groups", "tile")),
            P(("groups", "tile")),
        ),
        out_specs=P(("groups", "tile"), None, None, None),
        check_vma=False,
    )
```

```python
import jax
import numpy as np
import jax.numpy as jnp
from jax import lax
from jax.sharding import PartitionSpec as P


TX = 2


EPSILON = 1e-06

DIRECTIONS = ((1, 0), (-1, 0), (0, 1), (0, -1), (1, 1), (-1, -1), (1, -1), (-1, 1))


def activate(values, norm_gain, valid_cells):
    square = jnp.mean(values * values, axis=-1, keepdims=True)
    scaled = values * lax.rsqrt(square + EPSILON) * norm_gain
    return (jax.nn.silu(scaled) * valid_cells[..., None]).astype(jnp.bfloat16)


def latent_step(block, frame_tiles):
    length = lax.axis_size("tile")
    route = [(i, i + frame_tiles) for i in range(length - frame_tiles)]
    return lax.ppermute(block, "tile", route)


def direction_pairs(frame_tiles, step):
    length = lax.axis_size("tile")
    tile_rows = frame_tiles // TX
    step_rows, step_cols = step
    pairs = []
    for i in range(length):
        latent, rest = divmod(i, frame_tiles)
        ty, tx = divmod(rest, TX)
        ty2, tx2 = ty + step_rows, tx + step_cols
        if 0 <= ty2 < tile_rows and 0 <= tx2 < TX:
            pairs.append((i, latent * frame_tiles + ty2 * TX + tx2))
    return pairs


def direction_groups(frame_tiles):
    groups = []
    for step in DIRECTIONS:
        pairs = direction_pairs(frame_tiles, step)
        kind = (abs(step[0]), abs(step[1]))
        for group in groups:
            if group["kind"] != kind:
                continue
            sources = {s for s, _ in group["pairs"]}
            targets = {t for _, t in group["pairs"]}
            if sources.isdisjoint(s for s, _ in pairs) and targets.isdisjoint(t for _, t in pairs):
                group["steps"].append(step)
                group["pairs"] = group["pairs"] + pairs
                break
        else:
            groups.append({"kind": kind, "steps": [step], "pairs": pairs})
    return groups


def in_frame(ty, tx, tile_rows):
    return (ty >= 0) & (ty < tile_rows) & (tx >= 0) & (tx < TX)


def halo_pieces(cells, frame_tiles, latents_ahead):
    length = lax.axis_size("tile")
    tile_rows = frame_tiles // TX
    position = lax.axis_index("tile")
    ty = position % frame_tiles // TX
    tx = position % TX
    height, breadth, channels = cells.shape
    ahead = latents_ahead * frame_tiles
    received = {}
    for group in direction_groups(frame_tiles):
        steps = group["steps"]
        row_at = jnp.int32(0)
        col_at = jnp.int32(0)
        for step in steps:
            sends = in_frame(ty + step[0], tx + step[1], tile_rows)
            row_at = jnp.where(sends, height - 1 if step[0] == 1 else 0, row_at)
            col_at = jnp.where(sends, breadth - 1 if step[1] == 1 else 0, col_at)
        sizes = (1 if steps[0][0] else height, 1 if steps[0][1] else breadth, channels)
        piece = lax.dynamic_slice(cells, (row_at, col_at, jnp.int32(0)), sizes)
        pairs = [(s, t + ahead) for s, t in group["pairs"] if t + ahead < length]
        got = lax.ppermute(piece, "tile", pairs)
        for step in steps:
            if len(steps) == 1:
                received[step] = got
            else:
                gets = in_frame(ty - step[0], tx - step[1], tile_rows)
                received[step] = jnp.where(gets, got, jnp.zeros_like(got))
    return received


def with_halo(cells, received):
    upper = jnp.concatenate([received[(1, 1)], received[(1, 0)], received[(1, -1)]], axis=1)
    middle = jnp.concatenate([received[(0, 1)], cells, received[(0, -1)]], axis=1)
    lower = jnp.concatenate([received[(-1, 1)], received[(-1, 0)], received[(-1, -1)]], axis=1)
    return jnp.concatenate([upper, middle, lower], axis=0)


def halo_exchange(cells, frame_tiles):
    return with_halo(cells, halo_pieces(cells, frame_tiles, 0))


def conv2d(widened, kernel):
    return lax.conv_general_dilated(
        widened[None],
        kernel,
        (1, 1),
        "VALID",
        dimension_numbers=("NHWC", "HWIO", "NHWC"),
        preferred_element_type=jnp.float32,
    )[0]


def up_kernels(up_weight):
    channels, taps_y, taps_x, out_channels = up_weight.shape
    row_taps = ((3, 1), (2, 0))
    col_taps = ((3, None), (1, 2), (None, 0))
    select = np.zeros((2, 2, 3, taps_y * taps_x, 2), np.float32)
    for row_par in range(2):
        for a, ky in enumerate(row_taps[row_par]):
            for b, kx_pair in enumerate(col_taps):
                for col_par, kx in enumerate(kx_pair):
                    if kx is not None:
                        select[row_par, a, b, ky * taps_x + kx, col_par] = 1.0
    select = jnp.asarray(select.reshape(12, taps_y * taps_x, 2), up_weight.dtype)
    flat = up_weight.reshape(channels, taps_y * taps_x, out_channels)
    picked = jnp.einsum("qkr,ckd->qcrd", select, flat, preferred_element_type=jnp.float32)
    picked = picked.astype(up_weight.dtype).reshape(2, 2, 3, channels, 2 * out_channels)
    return [picked[0], picked[1]]


def body(
    frames, norm_gain, conv_weight, conv_bias, up_weight, up_bias, continues, row_extent, col_extent
):
    latents = continues.shape[0]
    frame_tiles = lax.axis_size("tile") // latents
    position = lax.axis_index("tile")
    latent_id = position // frame_tiles
    height = frames.shape[1]
    breadth = frames.shape[2]
    out_channels = up_weight.shape[3]
    rows_in = row_extent[0]
    cols_in = col_extent[0]
    row_ids = jnp.arange(height, dtype=jnp.int32)
    col_ids = jnp.arange(breadth, dtype=jnp.int32)
    valid_cells = ((row_ids[:, None] < rows_in) & (col_ids[None, :] < cols_in)).astype(jnp.float32)
    wide_rows = jnp.arange(-1, height + 1, dtype=jnp.int32)
    wide_cols = jnp.arange(-1, breadth + 1, dtype=jnp.int32)
    row_ok = (wide_rows < rows_in) | ((wide_rows == height) & (rows_in == height))
    col_ok = (wide_cols < cols_in) | ((wide_cols == breadth) & (cols_in == breadth))
    wide_valid = (row_ok[:, None] & col_ok[None, :]).astype(jnp.float32)

    raw = frames[0]
    raw_last = latent_step(raw, frame_tiles)
    halo_own = halo_pieces(raw, frame_tiles, 0)
    kernels = up_kernels(up_weight)
    raw_wide = with_halo(raw, halo_own)
    raw_wide, own_gain, own_valid = lax.optimization_barrier((raw_wide, norm_gain, wide_valid))
    active = activate(raw_wide.astype(jnp.float32), own_gain, own_valid)
    conv_own = lax.optimization_barrier(conv2d(active, conv_weight[2]))
    raw_before = latent_step(raw_last, frame_tiles)
    halo_last = halo_pieces(raw_last, frame_tiles, 0)
    last_wide = with_halo(raw_last, halo_last)
    last_frame = activate(last_wide.astype(jnp.float32), norm_gain, wide_valid)
    conv_last = conv2d(last_frame, conv_weight[1]) + conv_own

    slots = jnp.arange(latents, dtype=jnp.int32)
    flag_second = jnp.sum(jnp.where(slots == latent_id, continues, 0)).astype(jnp.bfloat16)
    before_wide = with_halo(raw_before, halo_pieces(raw_before, frame_tiles, 0))
    before = activate(before_wide.astype(jnp.float32), norm_gain, wide_valid) * flag_second
    conv_out = conv2d(before, conv_weight[0]) + conv_last

    values = raw.astype(jnp.float32)
    hidden = ((values + conv_out + conv_bias) * valid_cells[..., None]).astype(jnp.bfloat16)
    hidden_wide = halo_exchange(hidden, frame_tiles)
    bias_pair = jnp.concatenate([up_bias, up_bias])
    planes = []
    for row_par in range(2):
        summed = conv2d(hidden_wide[row_par : row_par + height + 1], kernels[row_par])
        planes.append(((summed + bias_pair) * valid_cells[..., None]).astype(jnp.bfloat16))
    woven = jnp.stack(planes, axis=1)
    upsampled = woven.reshape(2 * height, 2 * breadth, out_channels)
    return upsampled[None]


def solution(mesh):
    return jax.shard_map(
        body,
        mesh=mesh,
        in_specs=(
            P(("groups", "tile"), None, None, None),
            P(),
            P(),
            P(),
            P(),
            P(),
            P("groups"),
            P(("groups", "tile")),
            P(("groups", "tile")),
        ),
        out_specs=P(("groups", "tile"), None, None, None),
        check_vma=False,
    )
```

```python
import jax
import numpy as np
import jax.numpy as jnp
from jax import lax
from jax.sharding import PartitionSpec as P


TX = 2


EPSILON = 1e-06

DIRECTIONS = ((1, 0), (-1, 0), (0, 1), (0, -1), (1, 1), (-1, -1), (1, -1), (-1, 1))


def activate(values, norm_gain, valid_cells):
    square = jnp.mean(values * values, axis=-1, keepdims=True)
    scaled = values * lax.rsqrt(square + EPSILON) * norm_gain
    return (jax.nn.silu(scaled) * valid_cells[..., None]).astype(jnp.bfloat16)


def latent_step(block, frame_tiles):
    length = lax.axis_size("tile")
    route = [(i, i + frame_tiles) for i in range(length - frame_tiles)]
    return lax.ppermute(block, "tile", route)


def direction_pairs(frame_tiles, step):
    length = lax.axis_size("tile")
    tile_rows = frame_tiles // TX
    step_rows, step_cols = step
    pairs = []
    for i in range(length):
        latent, rest = divmod(i, frame_tiles)
        ty, tx = divmod(rest, TX)
        ty2, tx2 = ty + step_rows, tx + step_cols
        if 0 <= ty2 < tile_rows and 0 <= tx2 < TX:
            pairs.append((i, latent * frame_tiles + ty2 * TX + tx2))
    return pairs


def direction_groups(frame_tiles):
    groups = []
    for step in DIRECTIONS:
        pairs = direction_pairs(frame_tiles, step)
        kind = (abs(step[0]), abs(step[1]))
        for group in groups:
            if group["kind"] != kind:
                continue
            sources = {s for s, _ in group["pairs"]}
            targets = {t for _, t in group["pairs"]}
            if sources.isdisjoint(s for s, _ in pairs) and targets.isdisjoint(t for _, t in pairs):
                group["steps"].append(step)
                group["pairs"] = group["pairs"] + pairs
                break
        else:
            groups.append({"kind": kind, "steps": [step], "pairs": pairs})
    return groups


def in_frame(ty, tx, tile_rows):
    return (ty >= 0) & (ty < tile_rows) & (tx >= 0) & (tx < TX)


def halo_pieces(cells, frame_tiles, latents_ahead, width=1):
    length = lax.axis_size("tile")
    tile_rows = frame_tiles // TX
    position = lax.axis_index("tile")
    ty = position % frame_tiles // TX
    tx = position % TX
    height, breadth, channels = cells.shape
    ahead = latents_ahead * frame_tiles
    received = {}
    for group in direction_groups(frame_tiles):
        steps = group["steps"]
        row_at = jnp.int32(0)
        col_at = jnp.int32(0)
        for step in steps:
            sends = in_frame(ty + step[0], tx + step[1], tile_rows)
            row_at = jnp.where(sends, height - width if step[0] == 1 else 0, row_at)
            col_at = jnp.where(sends, breadth - width if step[1] == 1 else 0, col_at)
        sizes = (width if steps[0][0] else height, width if steps[0][1] else breadth, channels)
        piece = lax.dynamic_slice(cells, (row_at, col_at, jnp.int32(0)), sizes)
        pairs = [(s, t + ahead) for s, t in group["pairs"] if t + ahead < length]
        got = lax.ppermute(piece, "tile", pairs)
        for step in steps:
            if len(steps) == 1:
                received[step] = got
            else:
                gets = in_frame(ty - step[0], tx - step[1], tile_rows)
                received[step] = jnp.where(gets, got, jnp.zeros_like(got))
    return received


def with_halo(cells, received):
    upper = jnp.concatenate([received[(1, 1)], received[(1, 0)], received[(1, -1)]], axis=1)
    middle = jnp.concatenate([received[(0, 1)], cells, received[(0, -1)]], axis=1)
    lower = jnp.concatenate([received[(-1, 1)], received[(-1, 0)], received[(-1, -1)]], axis=1)
    return jnp.concatenate([upper, middle, lower], axis=0)


def conv2d(widened, kernel):
    return lax.conv_general_dilated(
        widened[None],
        kernel,
        (1, 1),
        "VALID",
        dimension_numbers=("NHWC", "HWIO", "NHWC"),
        preferred_element_type=jnp.float32,
    )[0]


def up_kernels(up_weight):
    channels, taps_y, taps_x, out_channels = up_weight.shape
    row_taps = ((3, 1), (2, 0))
    col_taps = ((3, None), (1, 2), (None, 0))
    select = np.zeros((2, 2, 3, taps_y * taps_x, 2), np.float32)
    for row_par in range(2):
        for a, ky in enumerate(row_taps[row_par]):
            for b, kx_pair in enumerate(col_taps):
                for col_par, kx in enumerate(kx_pair):
                    if kx is not None:
                        select[row_par, a, b, ky * taps_x + kx, col_par] = 1.0
    select = jnp.asarray(select.reshape(12, taps_y * taps_x, 2), up_weight.dtype)
    flat = up_weight.reshape(channels, taps_y * taps_x, out_channels)
    picked = jnp.einsum("qkr,ckd->qcrd", select, flat, preferred_element_type=jnp.float32)
    picked = picked.astype(up_weight.dtype).reshape(2, 2, 3, channels, 2 * out_channels)
    return [picked[0], picked[1]]


def body(
    frames, norm_gain, conv_weight, conv_bias, up_weight, up_bias, continues, row_extent, col_extent
):
    latents = continues.shape[0]
    frame_tiles = lax.axis_size("tile") // latents
    position = lax.axis_index("tile")
    latent_id = position // frame_tiles
    height = frames.shape[1]
    breadth = frames.shape[2]
    out_channels = up_weight.shape[3]
    rows_in = row_extent[0]
    cols_in = col_extent[0]
    tile_rows = frame_tiles // TX
    ty = position % frame_tiles // TX
    tx = position % TX
    row_ids = jnp.arange(height, dtype=jnp.int32)
    col_ids = jnp.arange(breadth, dtype=jnp.int32)
    valid_cells = ((row_ids[:, None] < rows_in) & (col_ids[None, :] < cols_in)).astype(jnp.float32)
    act_valid = jnp.pad(valid_cells, 2, constant_values=1.0)
    ring_rows = jnp.arange(-1, height + 1, dtype=jnp.int32)
    ring_cols = jnp.arange(-1, breadth + 1, dtype=jnp.int32)
    row_ok = jnp.where(
        ring_rows < 0, ty > 0, jnp.where(ring_rows >= height, ty < tile_rows - 1, ring_rows < rows_in)
    )
    col_ok = jnp.where(
        ring_cols < 0, tx > 0, jnp.where(ring_cols >= breadth, tx < TX - 1, ring_cols < cols_in)
    )
    ring_valid = (row_ok[:, None] & col_ok[None, :]).astype(jnp.float32)
    mask_bf16 = valid_cells.astype(jnp.bfloat16)[..., None]

    def exchange(cells):
        return with_halo(cells, halo_pieces(cells * mask_bf16, frame_tiles, 0, 2))

    raw = frames[0]
    raw_last = latent_step(raw, frame_tiles)
    own_raw, own_mask = lax.optimization_barrier((raw, mask_bf16))
    halo_own = halo_pieces(own_raw * own_mask, frame_tiles, 0, 2)
    kernels = up_kernels(up_weight)
    raw_wide = with_halo(raw, halo_own)
    raw_wide, own_gain, own_valid = lax.optimization_barrier((raw_wide, norm_gain, act_valid))
    active = activate(raw_wide.astype(jnp.float32), own_gain, own_valid)
    conv_own = lax.optimization_barrier(conv2d(active, conv_weight[2]))
    raw_before = latent_step(raw_last, frame_tiles)
    last_raw, last_mask = lax.optimization_barrier((raw_last, mask_bf16))
    halo_last = halo_pieces(last_raw * last_mask, frame_tiles, 0, 2)
    last_wide = with_halo(raw_last, halo_last)
    last_frame = activate(last_wide.astype(jnp.float32), norm_gain, act_valid)
    conv_last = lax.optimization_barrier(conv2d(last_frame, conv_weight[1]) + conv_own)

    slots = jnp.arange(latents, dtype=jnp.int32)
    flag_second = jnp.sum(jnp.where(slots == latent_id, continues, 0)).astype(jnp.bfloat16)
    before_wide = exchange(raw_before)
    before = activate(before_wide.astype(jnp.float32), norm_gain, act_valid) * flag_second
    conv_out = conv2d(before, conv_weight[0]) + conv_last

    values = raw_wide[1:-1, 1:-1].astype(jnp.float32)
    hidden_wide = ((values + conv_out + conv_bias) * ring_valid[..., None]).astype(jnp.bfloat16)
    bias_pair = jnp.concatenate([up_bias, up_bias])
    planes = []
    for row_par in range(2):
        summed = conv2d(hidden_wide[row_par : row_par + height + 1], kernels[row_par])
        planes.append(((summed + bias_pair) * valid_cells[..., None]).astype(jnp.bfloat16))
    woven = jnp.stack(planes, axis=1)
    upsampled = woven.reshape(2 * height, 2 * breadth, out_channels)
    return upsampled[None]


def solution(mesh):
    return jax.shard_map(
        body,
        mesh=mesh,
        in_specs=(
            P(("groups", "tile"), None, None, None),
            P(),
            P(),
            P(),
            P(),
            P(),
            P("groups"),
            P(("groups", "tile")),
            P(("groups", "tile")),
        ),
        out_specs=P(("groups", "tile"), None, None, None),
        check_vma=False,
    )
```

```python
import jax
import numpy as np
import jax.numpy as jnp
from jax import lax
from jax.sharding import PartitionSpec as P


TX = 2


EPSILON = 1e-06

DIRECTIONS = ((1, 0), (-1, 0), (0, 1), (0, -1), (1, 1), (-1, -1), (1, -1), (-1, 1))


def activate(values, norm_gain, valid_cells):
    square = jnp.mean(values * values, axis=-1, keepdims=True)
    scaled = values * lax.rsqrt(square + EPSILON) * norm_gain
    return (jax.nn.silu(scaled) * valid_cells[..., None]).astype(jnp.bfloat16)


def latent_step(block, frame_tiles):
    length = lax.axis_size("tile")
    route = [(i, i + frame_tiles) for i in range(length - frame_tiles)]
    return lax.ppermute(block, "tile", route)


def direction_pairs(frame_tiles, step):
    length = lax.axis_size("tile")
    tile_rows = frame_tiles // TX
    step_rows, step_cols = step
    pairs = []
    for i in range(length):
        latent, rest = divmod(i, frame_tiles)
        ty, tx = divmod(rest, TX)
        ty2, tx2 = ty + step_rows, tx + step_cols
        if 0 <= ty2 < tile_rows and 0 <= tx2 < TX:
            pairs.append((i, latent * frame_tiles + ty2 * TX + tx2))
    return pairs


def direction_groups(frame_tiles):
    groups = []
    for step in DIRECTIONS:
        pairs = direction_pairs(frame_tiles, step)
        kind = (abs(step[0]), abs(step[1]))
        for group in groups:
            if group["kind"] != kind:
                continue
            sources = {s for s, _ in group["pairs"]}
            targets = {t for _, t in group["pairs"]}
            if sources.isdisjoint(s for s, _ in pairs) and targets.isdisjoint(t for _, t in pairs):
                group["steps"].append(step)
                group["pairs"] = group["pairs"] + pairs
                break
        else:
            groups.append({"kind": kind, "steps": [step], "pairs": pairs})
    return groups


def in_frame(ty, tx, tile_rows):
    return (ty >= 0) & (ty < tile_rows) & (tx >= 0) & (tx < TX)


def halo_pieces(cells, frame_tiles, latents_ahead, width=1):
    length = lax.axis_size("tile")
    tile_rows = frame_tiles // TX
    position = lax.axis_index("tile")
    ty = position % frame_tiles // TX
    tx = position % TX
    height, breadth, channels = cells.shape
    ahead = latents_ahead * frame_tiles
    received = {}
    for group in direction_groups(frame_tiles):
        steps = group["steps"]
        row_at = jnp.int32(0)
        col_at = jnp.int32(0)
        for step in steps:
            sends = in_frame(ty + step[0], tx + step[1], tile_rows)
            row_at = jnp.where(sends, height - width if step[0] == 1 else 0, row_at)
            col_at = jnp.where(sends, breadth - width if step[1] == 1 else 0, col_at)
        sizes = (width if steps[0][0] else height, width if steps[0][1] else breadth, channels)
        piece = lax.dynamic_slice(cells, (row_at, col_at, jnp.int32(0)), sizes)
        pairs = [(s, t + ahead) for s, t in group["pairs"] if t + ahead < length]
        got = lax.ppermute(piece, "tile", pairs)
        for step in steps:
            if len(steps) == 1:
                received[step] = got
            else:
                gets = in_frame(ty - step[0], tx - step[1], tile_rows)
                received[step] = jnp.where(gets, got, jnp.zeros_like(got))
    return received


def with_halo(cells, received):
    upper = jnp.concatenate([received[(1, 1)], received[(1, 0)], received[(1, -1)]], axis=1)
    middle = jnp.concatenate([received[(0, 1)], cells, received[(0, -1)]], axis=1)
    lower = jnp.concatenate([received[(-1, 1)], received[(-1, 0)], received[(-1, -1)]], axis=1)
    return jnp.concatenate([upper, middle, lower], axis=0)


def conv2d(widened, kernel):
    return lax.conv_general_dilated(
        widened[None],
        kernel,
        (1, 1),
        "VALID",
        dimension_numbers=("NHWC", "HWIO", "NHWC"),
        preferred_element_type=jnp.float32,
    )[0]


def up_kernels(up_weight):
    channels, taps_y, taps_x, out_channels = up_weight.shape
    row_taps = ((3, 1), (2, 0))
    col_taps = ((3, None), (1, 2), (None, 0))
    select = np.zeros((2, 2, 3, taps_y * taps_x, 2), np.float32)
    for row_par in range(2):
        for a, ky in enumerate(row_taps[row_par]):
            for b, kx_pair in enumerate(col_taps):
                for col_par, kx in enumerate(kx_pair):
                    if kx is not None:
                        select[row_par, a, b, ky * taps_x + kx, col_par] = 1.0
    select = jnp.asarray(select.reshape(12, taps_y * taps_x, 2), up_weight.dtype)
    flat = up_weight.reshape(channels, taps_y * taps_x, out_channels)
    picked = jnp.einsum("qkr,ckd->qcrd", select, flat, preferred_element_type=jnp.float32)
    picked = picked.astype(up_weight.dtype).reshape(2, 2, 3, channels, 2 * out_channels)
    return [picked[0], picked[1]]


def body(
    frames, norm_gain, conv_weight, conv_bias, up_weight, up_bias, continues, row_extent, col_extent
):
    latents = continues.shape[0]
    frame_tiles = lax.axis_size("tile") // latents
    position = lax.axis_index("tile")
    latent_id = position // frame_tiles
    height = frames.shape[1]
    breadth = frames.shape[2]
    out_channels = up_weight.shape[3]
    rows_in = row_extent[0]
    cols_in = col_extent[0]
    tile_rows = frame_tiles // TX
    ty = position % frame_tiles // TX
    tx = position % TX
    row_ids = jnp.arange(height, dtype=jnp.int32)
    col_ids = jnp.arange(breadth, dtype=jnp.int32)
    valid_cells = ((row_ids[:, None] < rows_in) & (col_ids[None, :] < cols_in)).astype(jnp.float32)
    act_valid = jnp.pad(valid_cells, 2, constant_values=1.0)
    ring_rows = jnp.arange(-1, height + 1, dtype=jnp.int32)
    ring_cols = jnp.arange(-1, breadth + 1, dtype=jnp.int32)
    row_ok = jnp.where(
        ring_rows < 0, ty > 0, jnp.where(ring_rows >= height, ty < tile_rows - 1, ring_rows < rows_in)
    )
    col_ok = jnp.where(
        ring_cols < 0, tx > 0, jnp.where(ring_cols >= breadth, tx < TX - 1, ring_cols < cols_in)
    )
    ring_valid = (row_ok[:, None] & col_ok[None, :]).astype(jnp.float32)
    mask_bf16 = valid_cells.astype(jnp.bfloat16)[..., None]

    def exchange(cells):
        return with_halo(cells, halo_pieces(cells * mask_bf16, frame_tiles, 0, 2))

    raw = frames[0]
    raw_last = latent_step(raw, frame_tiles)
    own_raw, own_mask = lax.optimization_barrier((raw, mask_bf16))
    halo_own = halo_pieces(own_raw * own_mask, frame_tiles, 0, 2)
    kernels = up_kernels(up_weight)
    raw_wide = with_halo(raw, halo_own)
    raw_wide, own_gain, own_valid = lax.optimization_barrier((raw_wide, norm_gain, act_valid))
    active = activate(raw_wide.astype(jnp.float32), own_gain, own_valid)
    conv_own = lax.optimization_barrier(conv2d(active, conv_weight[2]))
    raw_before = latent_step(raw_last, frame_tiles)
    last_raw, last_mask = lax.optimization_barrier((raw_last, mask_bf16))
    halo_last = halo_pieces(last_raw * last_mask, frame_tiles, 0, 2)
    last_wide = with_halo(raw_last, halo_last)
    last_frame = activate(last_wide.astype(jnp.float32), norm_gain, act_valid)
    conv_last = lax.optimization_barrier(conv2d(last_frame, conv_weight[1]) + conv_own)

    slots = jnp.arange(latents, dtype=jnp.int32)
    flag_second = jnp.sum(jnp.where(slots == latent_id, continues, 0)).astype(jnp.bfloat16)
    before_wide = exchange(raw_before)
    before_wide, before_gain, before_valid = lax.optimization_barrier((before_wide, norm_gain, act_valid))
    before = activate(before_wide.astype(jnp.float32), before_gain, before_valid)
    conv_out = conv2d(before, conv_weight[0]) * flag_second.astype(jnp.float32) + conv_last

    values = raw_wide[1:-1, 1:-1].astype(jnp.float32)
    hidden_wide = ((values + conv_out + conv_bias) * ring_valid[..., None]).astype(jnp.bfloat16)
    bias_pair = jnp.concatenate([up_bias, up_bias])
    planes = []
    for row_par in range(2):
        summed = conv2d(hidden_wide[row_par : row_par + height + 1], kernels[row_par])
        planes.append(((summed + bias_pair) * valid_cells[..., None]).astype(jnp.bfloat16))
    woven = jnp.stack(planes, axis=1)
    upsampled = woven.reshape(2 * height, 2 * breadth, out_channels)
    return upsampled[None]


def solution(mesh):
    return jax.shard_map(
        body,
        mesh=mesh,
        in_specs=(
            P(("groups", "tile"), None, None, None),
            P(),
            P(),
            P(),
            P(),
            P(),
            P("groups"),
            P(("groups", "tile")),
            P(("groups", "tile")),
        ),
        out_specs=P(("groups", "tile"), None, None, None),
        check_vma=False,
    )
```

```python
import jax
import numpy as np
import jax.numpy as jnp
from jax import lax
from jax.sharding import PartitionSpec as P


TX = 2


EPSILON = 1e-06

DIRECTIONS = ((1, 0), (-1, 0), (0, 1), (0, -1), (1, 1), (-1, -1), (1, -1), (-1, 1))


def activate(values, norm_gain, valid_cells):
    square = jnp.mean(values * values, axis=-1, keepdims=True)
    scaled = values * lax.rsqrt(square + EPSILON) * norm_gain
    return (jax.nn.silu(scaled) * valid_cells[..., None]).astype(jnp.bfloat16)


def latent_step(block, frame_tiles):
    length = lax.axis_size("tile")
    route = [(i, i + frame_tiles) for i in range(length - frame_tiles)]
    return lax.ppermute(block, "tile", route)


def direction_pairs(frame_tiles, step):
    length = lax.axis_size("tile")
    tile_rows = frame_tiles // TX
    step_rows, step_cols = step
    pairs = []
    for i in range(length):
        latent, rest = divmod(i, frame_tiles)
        ty, tx = divmod(rest, TX)
        ty2, tx2 = ty + step_rows, tx + step_cols
        if 0 <= ty2 < tile_rows and 0 <= tx2 < TX:
            pairs.append((i, latent * frame_tiles + ty2 * TX + tx2))
    return pairs


def direction_groups(frame_tiles):
    groups = []
    for step in DIRECTIONS:
        pairs = direction_pairs(frame_tiles, step)
        kind = (abs(step[0]), abs(step[1]))
        for group in groups:
            if group["kind"] != kind:
                continue
            sources = {s for s, _ in group["pairs"]}
            targets = {t for _, t in group["pairs"]}
            if sources.isdisjoint(s for s, _ in pairs) and targets.isdisjoint(t for _, t in pairs):
                group["steps"].append(step)
                group["pairs"] = group["pairs"] + pairs
                break
        else:
            groups.append({"kind": kind, "steps": [step], "pairs": pairs})
    return groups


def in_frame(ty, tx, tile_rows):
    return (ty >= 0) & (ty < tile_rows) & (tx >= 0) & (tx < TX)


def halo_pieces(cells, frame_tiles, latents_ahead):
    length = lax.axis_size("tile")
    tile_rows = frame_tiles // TX
    position = lax.axis_index("tile")
    ty = position % frame_tiles // TX
    tx = position % TX
    height, breadth, channels = cells.shape
    ahead = latents_ahead * frame_tiles
    received = {}
    for group in direction_groups(frame_tiles):
        steps = group["steps"]
        row_at = jnp.int32(0)
        col_at = jnp.int32(0)
        for step in steps:
            sends = in_frame(ty + step[0], tx + step[1], tile_rows)
            row_at = jnp.where(sends, height - 1 if step[0] == 1 else 0, row_at)
            col_at = jnp.where(sends, breadth - 1 if step[1] == 1 else 0, col_at)
        sizes = (1 if steps[0][0] else height, 1 if steps[0][1] else breadth, channels)
        piece = lax.dynamic_slice(cells, (row_at, col_at, jnp.int32(0)), sizes)
        pairs = [(s, t + ahead) for s, t in group["pairs"] if t + ahead < length]
        got = lax.ppermute(piece, "tile", pairs)
        for step in steps:
            if len(steps) == 1:
                received[step] = got
            else:
                gets = in_frame(ty - step[0], tx - step[1], tile_rows)
                received[step] = jnp.where(gets, got, jnp.zeros_like(got))
    return received


def with_halo(cells, received):
    upper = jnp.concatenate([received[(1, 1)], received[(1, 0)], received[(1, -1)]], axis=1)
    middle = jnp.concatenate([received[(0, 1)], cells, received[(0, -1)]], axis=1)
    lower = jnp.concatenate([received[(-1, 1)], received[(-1, 0)], received[(-1, -1)]], axis=1)
    return jnp.concatenate([upper, middle, lower], axis=0)


def halo_exchange(cells, frame_tiles):
    return with_halo(cells, halo_pieces(cells, frame_tiles, 0))


def conv2d(widened, kernel):
    return lax.conv_general_dilated(
        widened[None],
        kernel,
        (1, 1),
        "VALID",
        dimension_numbers=("NHWC", "HWIO", "NHWC"),
        preferred_element_type=jnp.float32,
    )[0]


def up_kernels(up_weight):
    channels, taps_y, taps_x, out_channels = up_weight.shape
    row_taps = ((3, 1), (2, 0))
    col_taps = ((3, None), (1, 2), (None, 0))
    select = np.zeros((2, 2, 3, taps_y * taps_x, 2), np.float32)
    for row_par in range(2):
        for a, ky in enumerate(row_taps[row_par]):
            for b, kx_pair in enumerate(col_taps):
                for col_par, kx in enumerate(kx_pair):
                    if kx is not None:
                        select[row_par, a, b, ky * taps_x + kx, col_par] = 1.0
    select = jnp.asarray(select.reshape(12, taps_y * taps_x, 2), up_weight.dtype)
    flat = up_weight.reshape(channels, taps_y * taps_x, out_channels)
    picked = jnp.einsum("qkr,ckd->qcrd", select, flat, preferred_element_type=jnp.float32)
    picked = picked.astype(up_weight.dtype).reshape(2, 2, 3, channels, 2 * out_channels)
    return [picked[0], picked[1]]


def body(
    frames, norm_gain, conv_weight, conv_bias, up_weight, up_bias, continues, row_extent, col_extent
):
    latents = continues.shape[0]
    frame_tiles = lax.axis_size("tile") // latents
    position = lax.axis_index("tile")
    latent_id = position // frame_tiles
    height = frames.shape[1]
    breadth = frames.shape[2]
    out_channels = up_weight.shape[3]
    rows_in = row_extent[0]
    cols_in = col_extent[0]
    row_ids = jnp.arange(height, dtype=jnp.int32)
    col_ids = jnp.arange(breadth, dtype=jnp.int32)
    valid_cells = ((row_ids[:, None] < rows_in) & (col_ids[None, :] < cols_in)).astype(jnp.float32)
    wide_rows = jnp.arange(-1, height + 1, dtype=jnp.int32)
    wide_cols = jnp.arange(-1, breadth + 1, dtype=jnp.int32)
    row_ok = (wide_rows < rows_in) | ((wide_rows == height) & (rows_in == height))
    col_ok = (wide_cols < cols_in) | ((wide_cols == breadth) & (cols_in == breadth))
    wide_valid = (row_ok[:, None] & col_ok[None, :]).astype(jnp.float32)

    raw = frames[0]
    raw_last = latent_step(raw, frame_tiles)
    halo_own = halo_pieces(raw, frame_tiles, 0)
    kernels = up_kernels(up_weight)
    raw_wide = with_halo(raw, halo_own)
    raw_wide, own_gain, own_valid = lax.optimization_barrier((raw_wide, norm_gain, wide_valid))
    active = activate(raw_wide.astype(jnp.float32), own_gain, own_valid)
    pair_kernel = jnp.concatenate([conv_weight[2], conv_weight[1]], axis=2)
    active, pair_kernel = lax.optimization_barrier((active, pair_kernel))
    raw_before = latent_step(raw_last, frame_tiles)
    halo_last = halo_pieces(raw_last, frame_tiles, 0)
    last_wide = with_halo(raw_last, halo_last)
    last_frame = activate(last_wide.astype(jnp.float32), norm_gain, wide_valid)
    conv_last = conv2d(jnp.concatenate([active, last_frame], axis=-1), pair_kernel)

    slots = jnp.arange(latents, dtype=jnp.int32)
    flag_second = jnp.sum(jnp.where(slots == latent_id, continues, 0)).astype(jnp.bfloat16)
    before_wide = with_halo(raw_before, halo_pieces(raw_before, frame_tiles, 0))
    before = activate(before_wide.astype(jnp.float32), norm_gain, wide_valid) * flag_second
    conv_out = conv2d(before, conv_weight[0]) + conv_last

    values = raw.astype(jnp.float32)
    hidden = ((values + conv_out + conv_bias) * valid_cells[..., None]).astype(jnp.bfloat16)
    hidden_wide = halo_exchange(hidden, frame_tiles)
    bias_pair = jnp.concatenate([up_bias, up_bias])
    planes = []
    for row_par in range(2):
        summed = conv2d(hidden_wide[row_par : row_par + height + 1], kernels[row_par])
        planes.append(((summed + bias_pair) * valid_cells[..., None]).astype(jnp.bfloat16))
    woven = jnp.stack(planes, axis=1)
    upsampled = woven.reshape(2 * height, 2 * breadth, out_channels)
    return upsampled[None]


def solution(mesh):
    return jax.shard_map(
        body,
        mesh=mesh,
        in_specs=(
            P(("groups", "tile"), None, None, None),
            P(),
            P(),
            P(),
            P(),
            P(),
            P("groups"),
            P(("groups", "tile")),
            P(("groups", "tile")),
        ),
        out_specs=P(("groups", "tile"), None, None, None),
        check_vma=False,
    )
```

```python
import jax
import numpy as np
import jax.numpy as jnp
from jax import lax
from jax.sharding import PartitionSpec as P


TX = 2


EPSILON = 1e-06

DIRECTIONS = ((1, 0), (-1, 0), (0, 1), (0, -1), (1, 1), (-1, -1), (1, -1), (-1, 1))


def activate(values, norm_gain, valid_cells):
    square = jnp.mean(values * values, axis=-1, keepdims=True)
    scaled = values * lax.rsqrt(square + EPSILON) * norm_gain
    return (jax.nn.silu(scaled) * valid_cells[..., None]).astype(jnp.bfloat16)


def latent_step(block, frame_tiles):
    length = lax.axis_size("tile")
    route = [(i, i + frame_tiles) for i in range(length - frame_tiles)]
    return lax.ppermute(block, "tile", route)


def direction_pairs(frame_tiles, step):
    length = lax.axis_size("tile")
    tile_rows = frame_tiles // TX
    step_rows, step_cols = step
    pairs = []
    for i in range(length):
        latent, rest = divmod(i, frame_tiles)
        ty, tx = divmod(rest, TX)
        ty2, tx2 = ty + step_rows, tx + step_cols
        if 0 <= ty2 < tile_rows and 0 <= tx2 < TX:
            pairs.append((i, latent * frame_tiles + ty2 * TX + tx2))
    return pairs


def direction_groups(frame_tiles):
    groups = []
    for step in DIRECTIONS:
        pairs = direction_pairs(frame_tiles, step)
        kind = (abs(step[0]), abs(step[1]))
        for group in groups:
            if group["kind"] != kind:
                continue
            sources = {s for s, _ in group["pairs"]}
            targets = {t for _, t in group["pairs"]}
            if sources.isdisjoint(s for s, _ in pairs) and targets.isdisjoint(t for _, t in pairs):
                group["steps"].append(step)
                group["pairs"] = group["pairs"] + pairs
                break
        else:
            groups.append({"kind": kind, "steps": [step], "pairs": pairs})
    return groups


def in_frame(ty, tx, tile_rows):
    return (ty >= 0) & (ty < tile_rows) & (tx >= 0) & (tx < TX)


def halo_pieces(cells, frame_tiles, latents_ahead):
    length = lax.axis_size("tile")
    tile_rows = frame_tiles // TX
    position = lax.axis_index("tile")
    ty = position % frame_tiles // TX
    tx = position % TX
    height, breadth, channels = cells.shape
    ahead = latents_ahead * frame_tiles
    received = {}
    for group in direction_groups(frame_tiles):
        steps = group["steps"]
        row_at = jnp.int32(0)
        col_at = jnp.int32(0)
        for step in steps:
            sends = in_frame(ty + step[0], tx + step[1], tile_rows)
            row_at = jnp.where(sends, height - 1 if step[0] == 1 else 0, row_at)
            col_at = jnp.where(sends, breadth - 1 if step[1] == 1 else 0, col_at)
        sizes = (1 if steps[0][0] else height, 1 if steps[0][1] else breadth, channels)
        piece = lax.dynamic_slice(cells, (row_at, col_at, jnp.int32(0)), sizes)
        pairs = [(s, t + ahead) for s, t in group["pairs"] if t + ahead < length]
        got = lax.ppermute(piece, "tile", pairs)
        for step in steps:
            if len(steps) == 1:
                received[step] = got
            else:
                gets = in_frame(ty - step[0], tx - step[1], tile_rows)
                received[step] = jnp.where(gets, got, jnp.zeros_like(got))
    return received


def with_halo(cells, received):
    upper = jnp.concatenate([received[(1, 1)], received[(1, 0)], received[(1, -1)]], axis=1)
    middle = jnp.concatenate([received[(0, 1)], cells, received[(0, -1)]], axis=1)
    lower = jnp.concatenate([received[(-1, 1)], received[(-1, 0)], received[(-1, -1)]], axis=1)
    return jnp.concatenate([upper, middle, lower], axis=0)


def halo_exchange(cells, frame_tiles):
    return with_halo(cells, halo_pieces(cells, frame_tiles, 0))


def conv2d(widened, kernel):
    return lax.conv_general_dilated(
        widened[None],
        kernel,
        (1, 1),
        "VALID",
        dimension_numbers=("NHWC", "HWIO", "NHWC"),
        preferred_element_type=jnp.float32,
    )[0]


def up_kernels(up_weight):
    channels, taps_y, taps_x, out_channels = up_weight.shape
    row_taps = ((3, 1), (2, 0))
    col_taps = ((3, None), (1, 2), (None, 0))
    select = np.zeros((2, 2, 3, taps_y * taps_x, 2), np.float32)
    for row_par in range(2):
        for a, ky in enumerate(row_taps[row_par]):
            for b, kx_pair in enumerate(col_taps):
                for col_par, kx in enumerate(kx_pair):
                    if kx is not None:
                        select[row_par, a, b, ky * taps_x + kx, col_par] = 1.0
    select = jnp.asarray(select.reshape(12, taps_y * taps_x, 2), up_weight.dtype)
    flat = up_weight.reshape(channels, taps_y * taps_x, out_channels)
    picked = jnp.einsum("qkr,ckd->qcrd", select, flat, preferred_element_type=jnp.float32)
    picked = picked.astype(up_weight.dtype).reshape(2, 2, 3, channels, 2 * out_channels)
    return [picked[0], picked[1]]


def body(
    frames, norm_gain, conv_weight, conv_bias, up_weight, up_bias, continues, row_extent, col_extent
):
    latents = continues.shape[0]
    frame_tiles = lax.axis_size("tile") // latents
    position = lax.axis_index("tile")
    latent_id = position // frame_tiles
    height = frames.shape[1]
    breadth = frames.shape[2]
    out_channels = up_weight.shape[3]
    rows_in = row_extent[0]
    cols_in = col_extent[0]
    row_ids = jnp.arange(height, dtype=jnp.int32)
    col_ids = jnp.arange(breadth, dtype=jnp.int32)
    valid_cells = ((row_ids[:, None] < rows_in) & (col_ids[None, :] < cols_in)).astype(jnp.float32)
    wide_rows = jnp.arange(-1, height + 1, dtype=jnp.int32)
    wide_cols = jnp.arange(-1, breadth + 1, dtype=jnp.int32)
    row_ok = (wide_rows < rows_in) | ((wide_rows == height) & (rows_in == height))
    col_ok = (wide_cols < cols_in) | ((wide_cols == breadth) & (cols_in == breadth))
    wide_valid = (row_ok[:, None] & col_ok[None, :]).astype(jnp.float32)

    raw = frames[0]
    raw_last = latent_step(raw, frame_tiles)
    halo_own = halo_pieces(raw, frame_tiles, 0)
    kernels = up_kernels(up_weight)
    raw_wide = with_halo(raw, halo_own)
    raw_wide, own_gain, own_valid = lax.optimization_barrier((raw_wide, norm_gain, wide_valid))
    active = activate(raw_wide.astype(jnp.float32), own_gain, own_valid)
    pair_kernel = jnp.transpose(conv_weight[1:], (1, 2, 0, 3, 4))
    pair_kernel = pair_kernel.reshape(3, 3, -1, conv_weight.shape[-1])
    active, pair_kernel = lax.optimization_barrier((active, pair_kernel))
    raw_before = latent_step(raw_last, frame_tiles)
    halo_last = halo_pieces(raw_last, frame_tiles, 0)
    last_wide = with_halo(raw_last, halo_last)
    last_frame = activate(last_wide.astype(jnp.float32), norm_gain, wide_valid)
    conv_last = conv2d(jnp.concatenate([last_frame, active], axis=-1), pair_kernel)

    slots = jnp.arange(latents, dtype=jnp.int32)
    flag_second = jnp.sum(jnp.where(slots == latent_id, continues, 0)).astype(jnp.bfloat16)
    halo_before = halo_pieces(raw_before, frame_tiles, 0)
    before_wide = with_halo(raw_before, halo_before)
    before = activate(before_wide.astype(jnp.float32), norm_gain, wide_valid) * flag_second
    conv_out = conv2d(before, conv_weight[0]) + conv_last

    values = raw.astype(jnp.float32)
    hidden = ((values + conv_out + conv_bias) * valid_cells[..., None]).astype(jnp.bfloat16)
    hidden_wide = halo_exchange(hidden, frame_tiles)
    bias_pair = jnp.concatenate([up_bias, up_bias])
    planes = []
    for row_par in range(2):
        summed = conv2d(hidden_wide[row_par : row_par + height + 1], kernels[row_par])
        planes.append(((summed + bias_pair) * valid_cells[..., None]).astype(jnp.bfloat16))
    woven = jnp.stack(planes, axis=1)
    upsampled = woven.reshape(2 * height, 2 * breadth, out_channels)
    return upsampled[None]


def solution(mesh):
    return jax.shard_map(
        body,
        mesh=mesh,
        in_specs=(
            P(("groups", "tile"), None, None, None),
            P(),
            P(),
            P(),
            P(),
            P(),
            P("groups"),
            P(("groups", "tile")),
            P(("groups", "tile")),
        ),
        out_specs=P(("groups", "tile"), None, None, None),
        check_vma=False,
    )
```
